512 devices in a mesh: ctx: 64 (over z, x), ch: 8 (over y, core).
Axes of the slice: x: 4, y: 4, z: 16, core: 2. Of those that a mesh axis runs over, the one named last changes fastest.
Arguments:
- projections: bfloat16 [3, 16384, 8192], P(None, ('ctx', 'ch')), may hold values from -3 to 3
- attention_order: int32 [16384], replicated, may hold values from 0 to 16383, as said below
- doc_lengths: int32 [4], replicated, may hold values from 1 to 8192, 16384 in all
- short_filter: float32 [3, 3, 8192], P(None, None, 'ch'), may hold values from -3.5 to 3.5
- decay_rate: float32 [512, 16], P('ch'), may hold values from 6.1035157e-06 to 0.03
- residue: float32 [512, 16], P('ch'), may hold values from -1.5 to 1.5
- skip_gain: float32 [8192], P('ch'), may hold values from -2.5 to 2.5
Outputs:
- mixed_rows: bfloat16 [16384, 8192], P(('ctx', 'ch'))
The draws below stay inside these ranges and needn't reach their ends.
Inputs may be any that keep to these rules, and one draw needn't show every extreme that they name: `attention_order`: A permutation of the 16384 positions. For every group a of 256 rows (rows a * 256 to (a + 1) * 256 - 1) and every context block j, the rows a * 256 + j * 4 to a * 256 + (j + 1) * 4 - 1 hold positions of block j, that is j * 256 to (j + 1) * 256 - 1, in any order. `doc_lengths`: the documents lie one after another in the slab; the lengths sum to 16384.
All inputs are finite; a program needn't handle non-finite values.
Results may differ from the reference program's by a relative error of at most 0.0049.
Values may be sent and summed in bfloat16 or wider, within the bound.
No kernel may reach another device: no remote copies, remote signals or barrier semaphores. Data moves between devices by JAX's collectives and lax.ppermute only.
A program may use at most 64 MiB of HBM per device.

```python
import math
import jax
import jax.numpy as jnp
import numpy as np
from jax import lax

D = 8192
MODES = 16
FILTER_CHANNELS = 16
DOCS = 4
TOK_DEV = 256
TOKENS = 16384
FILTERS = 512


def draw_attention_order(key, part):
    block_total = TOKENS // TOK_DEV
    slot_rows = TOK_DEV // block_total
    subkeys = jax.random.split(key, block_total)
    shuffled = jax.vmap(lambda subkey: jax.random.permutation(subkey, TOK_DEV))(subkeys).astype(jnp.int32)
    positions = shuffled + (jnp.arange(block_total, dtype=jnp.int32) * TOK_DEV)[:, None]
    arranged = jnp.transpose(positions.reshape(block_total, block_total, slot_rows), (1, 0, 2))
    return arranged.reshape(TOKENS).astype(jnp.int32)


def levels(rng, dims, cuts, least, high):
    def one(axis_at, shards_of):
        draws = jax.random.uniform(jax.random.fold_in(jax.random.fold_in(rng, 6), axis_at), (shards_of,), jnp.float32, least / len(cuts), high / len(cuts))
        return jnp.repeat(jnp.exp(draws), dims[axis_at] // shards_of).reshape((-1,) + (1,) * (len(dims) - axis_at - 1))

    factor_of = one(*cuts[0])
    for cut in cuts[1:]:
        factor_of = factor_of * one(*cut)
    return factor_of


def split_up(amount, total, limit, skew):
    loads = [(1 << 20) // math.isqrt(grade ** skew) + 1 for grade in range(2, amount + 1)]
    surplus, holding = total - limit - (amount - 1), [1] * (amount - 1)
    while surplus > 0:
        candidates = [i for i in range(amount - 1) if holding[i] < limit]
        pool, budget = sum([loads[i] for i in candidates]), surplus
        for i in candidates:
            more = min(limit - holding[i], max(1, budget * loads[i] // pool), surplus)
            holding[i] = holding[i] + more
            surplus = surplus - more
    return np.array([limit] + holding)


def uneven_parts(own_key, amount, total, bound, skew):
    if amount == 2:
        one = jax.random.randint(own_key, (), max(1, total - bound), min(bound, total - 1) + 1)
        return jnp.stack([one, total - one])
    tallies = jnp.asarray(split_up(amount, total, bound, skew), jnp.int32)
    couples = (amount - 1) // 2
    giver, sink = tallies[1:1 + 2 * couples:2], tallies[2:2 + 2 * couples:2]
    margin = jnp.minimum(giver - 1, bound - sink)
    moved = jax.random.randint(jax.random.fold_in(own_key, 1), (couples,), 0, 1 << 20) % (margin + 1)
    tallies = tallies.at[1:1 + 2 * couples:2].set(giver - moved).at[2:2 + 2 * couples:2].set(sink + moved)
    return tallies[jax.random.permutation(jax.random.fold_in(own_key, 2), amount)]


def scatter_about(stream_key, shape, width, limit, pieces=(), held_as=jnp.bfloat16):
    factor_of = levels(stream_key, shape, pieces, -0.22, 0.18) if pieces else 1.0
    array = jax.random.normal(stream_key, shape, jnp.float32) * width * factor_of
    return jnp.minimum(jnp.maximum(array, -limit), limit).astype(held_as)


def setup_inputs(seed: int = 0) -> dict:
    seeds = jax.random.split(jax.random.key(seed), 8)
    projections = scatter_about(seeds[0], (3, TOKENS, D), 1.0, 3.0, ((1, 512),))
    attention_order = draw_attention_order(jax.random.fold_in(seeds[7], 71), 0)
    doc_lengths = uneven_parts(seeds[2], DOCS, TOKENS, TOKENS // 2, 2).astype(jnp.int32)
    short_filter = scatter_about(seeds[3], (3, 3, D), 3 ** -0.5, 3.5, ((2, 8),), jnp.float32)
    decay_rate = jnp.clip(jnp.exp(math.log(0.03) - 8.500088 * jax.random.uniform(seeds[4], (FILTERS, MODES), jnp.float32) ** levels(seeds[4], (FILTERS, MODES), ((0, 8),), -0.2, 0.2)), 6.10351571594947e-06, 0.03)
    residue = scatter_about(seeds[5], (FILTERS, MODES), 0.25, 1.5, ((0, 8),), jnp.float32)
    skip_gain = scatter_about(seeds[6], (D,), 1.0, 2.5, ((0, 8),), jnp.float32)
    return dict(projections=projections, attention_order=attention_order, doc_lengths=doc_lengths, short_filter=short_filter, decay_rate=decay_rate, residue=residue, skip_gain=skip_gain)


def reference(projections, attention_order, doc_lengths, short_filter, decay_rate, residue, skip_gain):
    positions = jnp.arange(TOKENS, dtype=jnp.int32)
    inverse = jnp.zeros((TOKENS,), jnp.int32).at[attention_order].set(positions)
    bounds = jnp.cumsum(doc_lengths).astype(jnp.int32)
    document = lax.optimization_barrier(jnp.sum((positions[:, None] >= bounds[None, :]).astype(jnp.int32), axis=1)).astype(jnp.int32)
    coefficient = residue * jnp.sqrt(1.0 - jnp.exp(-2.0 * decay_rate))
    decay_wide = jnp.repeat(jnp.exp(-decay_rate).T, FILTER_CHANNELS, axis=1)
    coeff_wide = jnp.repeat(coefficient.T, FILTER_CHANNELS, axis=1)

    def advance(carry, inputs):
        state, back_one, back_two, doc_one, doc_two = carry
        source, doc_now = inputs
        current_row = lax.dynamic_slice_in_dim(projections, source.astype(jnp.int32), 1, 1)[:, 0, :].astype(jnp.float32)
        keep_one = (doc_one == doc_now).astype(jnp.float32)
        keep_two = (doc_two == doc_now).astype(jnp.float32)
        featured = short_filter[:, 0, :] * current_row + short_filter[:, 1, :] * back_one * keep_one + short_filter[:, 2, :] * back_two * keep_two
        gated = (featured[1] * featured[2]).astype(jnp.bfloat16)
        gated_wide = lax.optimization_barrier(gated).astype(jnp.float32)
        state = decay_wide * state * keep_one + gated_wide[None, :]
        mixed = featured[0] * (lax.optimization_barrier(jnp.sum(coeff_wide * state, axis=0)) + skip_gain * gated_wide)
        return ((state, current_row, back_one, doc_now, doc_one), mixed.astype(jnp.bfloat16))
    initial = (jnp.zeros((MODES, D), jnp.float32), jnp.zeros((3, D), jnp.float32), jnp.zeros((3, D), jnp.float32), jnp.int32(-1), jnp.int32(-1))
    final_carry, mixed = lax.scan(advance, initial, (inverse, document))
    return jnp.take(mixed, attention_order, axis=0)
```

```python
import jax
import jax.numpy as jnp
from jax import lax
from jax.sharding import PartitionSpec as P

highest = lax.Precision.HIGHEST


def doc_index(positions, bounds):
    found = jnp.sum((positions[:, None] >= bounds[None, :]).astype(jnp.int32), axis=1)
    return jnp.where(positions >= 0, found, -1)


def shards(projections, attention_order, doc_lengths, short_filter, decay_rate, residue, skip_gain):
    n_ctx = lax.axis_size("ctx")
    n_ch = lax.axis_size("ch")
    here_ctx = lax.axis_index("ctx")
    here_ch = lax.axis_index("ch")
    feeds, rows_here, channels = projections.shape
    tokens = attention_order.shape[0]
    block = tokens // n_ctx
    slot = block // n_ctx
    chunks = rows_here // slot
    span = chunks * block
    width = channels // n_ctx
    local_groups, modes = decay_rate.shape
    local_channels = short_filter.shape[2]
    group_width = local_channels // local_groups
    groups = width // group_width
    n_docs = doc_lengths.shape[0]

    sizes = (short_filter.size, decay_rate.size, residue.size, skip_gain.size)
    flat = jnp.concatenate(
        [short_filter.reshape(-1), decay_rate.reshape(-1), residue.reshape(-1), skip_gain.reshape(-1)]
    )
    every = lax.all_gather(flat, "ch")
    o1 = sizes[0]
    o2 = o1 + sizes[1]
    o3 = o2 + sizes[2]
    sf_all = jnp.transpose(every[:, :o1].reshape(n_ch, 3, 3, local_channels), (1, 2, 0, 3)).reshape(
        3, 3, n_ch * local_channels
    )
    sf = lax.dynamic_slice_in_dim(sf_all, here_ctx * width, width, 2)
    rate = lax.dynamic_slice_in_dim(every[:, o1:o2].reshape(n_ch * local_groups, modes), here_ctx * groups, groups, 0)
    res = lax.dynamic_slice_in_dim(every[:, o2:o3].reshape(n_ch * local_groups, modes), here_ctx * groups, groups, 0)
    skip = lax.dynamic_slice_in_dim(every[:, o3:].reshape(n_ch * local_channels), here_ctx * width, width, 0)
    coefficient = res * jnp.sqrt(1.0 - jnp.exp(-2.0 * rate))

    received = lax.all_to_all(projections, "ctx", 2, 1, tiled=True)
    received = received.reshape(feeds, n_ctx, chunks, slot, width)
    received = jnp.transpose(received, (0, 2, 1, 3, 4)).reshape(feeds, chunks, n_ctx * slot, width)
    routing = attention_order.reshape(n_ctx, tokens // slot // n_ctx, slot)
    mine = lax.dynamic_slice_in_dim(routing, here_ch * chunks, chunks, 1)
    offsets = jnp.transpose(mine, (1, 0, 2)).reshape(chunks, n_ctx * slot)
    offsets = offsets - (here_ch * chunks + jnp.arange(chunks, dtype=jnp.int32))[:, None] * block
    placer = (offsets[:, None, :] == jnp.arange(block, dtype=jnp.int32)[None, :, None]).astype(jnp.bfloat16)
    ordered = jnp.einsum("kwr,pkrc->pkwc", placer, received, preferred_element_type=jnp.float32)
    ordered = ordered.astype(jnp.bfloat16).reshape(feeds, span, width)

    earlier = lax.ppermute(ordered[:, span - 2 :, :], "ch", [(i, i + 1) for i in range(n_ch - 1)])
    widened = jnp.concatenate([earlier, ordered], axis=1).astype(jnp.float32)
    bounds = jnp.cumsum(doc_lengths).astype(jnp.int32)
    span_docs = doc_index(here_ch * span - 2 + jnp.arange(span + 2, dtype=jnp.int32), bounds)
    current = span_docs[2:]
    keep_one = (span_docs[1 : 1 + span] == current).astype(jnp.float32)[None, :, None]
    keep_two = (span_docs[0:span] == current).astype(jnp.float32)[None, :, None]
    featured = (
        sf[:, 0, None, :] * widened[:, 2:]
        + sf[:, 1, None, :] * widened[:, 1 : 1 + span] * keep_one
        + sf[:, 2, None, :] * widened[:, 0:span] * keep_two
    )
    gated = (featured[1] * featured[2]).astype(jnp.bfloat16)

    steps = jnp.arange(block, dtype=jnp.float32)
    falling = coefficient[:, None, :] * jnp.exp(-rate[:, None, :] * steps[None, :, None])
    rising = jnp.exp(rate[:, :, None] * steps[None, None, :])
    lower = steps[:, None] >= steps[None, :]
    toeplitz = jnp.where(
        lower[None], jnp.einsum("gtm,gms->gts", falling, rising, precision=highest), 0.0
    )
    toe_hi = toeplitz.astype(jnp.bfloat16)
    toe_lo = (toeplitz - toe_hi.astype(jnp.float32)).astype(jnp.bfloat16)
    toe_both = jnp.concatenate([toe_hi, toe_lo], axis=2)
    x = gated.reshape(chunks, block, groups, group_width)
    docs_k = current.reshape(chunks, block)
    doc_ids = jnp.arange(n_docs, dtype=jnp.int32)
    in_doc = docs_k[None] == doc_ids[:, None, None]
    xd = jnp.where(in_doc[:, :, :, None, None], x[None], jnp.zeros((), jnp.bfloat16))
    xd = jnp.concatenate([xd, xd], axis=2)
    per_doc = jnp.einsum("gts,dksgc->dktgc", toe_both, xd, preferred_element_type=jnp.float32)
    intra = jnp.sum(jnp.where(in_doc[:, :, :, None, None], per_doc, 0.0), axis=0)

    x32 = x.astype(jnp.float32)
    ends_doc = docs_k[:, block - 1]
    at_end = (docs_k == ends_doc[:, None]).astype(jnp.float32)
    towards_end = jnp.exp(-rate[:, :, None] * (block - 1.0 - steps)[None, None, :])
    chunk_state = jnp.einsum(
        "gms,ksgc->kgmc", towards_end, x32 * at_end[:, :, None, None], precision=highest
    )
    chunk_ids = jnp.arange(chunks, dtype=jnp.int32)
    lag = (chunk_ids[:, None] - chunk_ids[None, :]).astype(jnp.float32)
    linked = (chunk_ids[:, None] >= chunk_ids[None, :]) & (ends_doc[:, None] == ends_doc[None, :])
    carry_weight = jnp.where(
        linked[:, :, None, None],
        jnp.exp(-rate[None, None] * (block * jnp.maximum(lag, 0.0))[:, :, None, None]),
        0.0,
    )
    local_state = jnp.sum(carry_weight[:, :, :, :, None] * chunk_state[None], axis=1)

    previous_doc = span_docs[1]
    span_factor = jnp.exp(-rate * float(span)) * (previous_doc == current[span - 1]).astype(jnp.float32)
    packed = jnp.concatenate([span_factor.reshape(-1), local_state[chunks - 1].reshape(-1)])
    gathered = lax.all_gather(packed, "ch")
    factors = gathered[:, : groups * modes].reshape(n_ch, groups, modes, 1)
    states = gathered[:, groups * modes :].reshape(n_ch, groups, modes, group_width)
    entering = jnp.zeros((groups, modes, group_width), jnp.float32)
    for source in range(n_ch):
        entering = jnp.where(source < here_ch, factors[source] * entering + states[source], entering)

    reach = jnp.exp(-rate[None] * (block * (chunk_ids + 1.0))[:, None, None])
    joined = (previous_doc == ends_doc).astype(jnp.float32)[:, None, None, None]
    total_state = local_state + reach[..., None] * joined * entering[None]
    before = jnp.concatenate([entering[None], total_state[: chunks - 1]], axis=0)
    start_prev_doc = jnp.concatenate([previous_doc[None], docs_k[: chunks - 1, block - 1]])
    from_before = (docs_k == start_prev_doc[:, None]).astype(jnp.float32)
    decaying = coefficient[:, None, :] * jnp.exp(-rate[:, None, :] * (steps + 1.0)[None, :, None])
    incoming = jnp.einsum("gtm,kgmc->ktgc", decaying, before, precision=highest)
    filtered = intra + incoming * from_before[:, :, None, None]

    gated32 = gated.astype(jnp.float32)
    combined = filtered.reshape(span, width) + skip[None, :] * gated32
    mixed = (featured[0] * combined).astype(jnp.bfloat16)

    back = jnp.einsum(
        "kwr,kwc->krc", placer, mixed.reshape(chunks, block, width), preferred_element_type=jnp.float32
    ).astype(jnp.bfloat16)
    back = jnp.transpose(back.reshape(chunks, n_ctx, slot, width), (1, 0, 2, 3)).reshape(
        n_ctx * rows_here, width
    )
    return lax.all_to_all(back, "ctx", 0, 1, tiled=True)


def solution(mesh):
    placed = (
        P(None, ("ctx", "ch"), None),
        P(),
        P(),
        P(None, None, "ch"),
        P("ch", None),
        P("ch", None),
        P("ch"),
    )
    return jax.shard_map(
        shards, mesh=mesh, in_specs=placed, out_specs=P(("ctx", "ch"), None), check_vma=False
    )
```

```python
import jax
import jax.numpy as jnp
from jax import lax
from jax.sharding import PartitionSpec as P

highest = lax.Precision.HIGHEST


def doc_index(positions, bounds):
    found = jnp.sum((positions[:, None] >= bounds[None, :]).astype(jnp.int32), axis=1)
    return jnp.where(positions >= 0, found, -1)


def shards(projections, attention_order, doc_lengths, short_filter, decay_rate, residue, skip_gain):
    n_ctx = lax.axis_size("ctx")
    n_ch = lax.axis_size("ch")
    here_ctx = lax.axis_index("ctx")
    here_ch = lax.axis_index("ch")
    feeds, rows_here, channels = projections.shape
    tokens = attention_order.shape[0]
    block = tokens // n_ctx
    slot = block // n_ctx
    chunks = rows_here // slot
    span = chunks * block
    width = channels // n_ctx
    local_groups, modes = decay_rate.shape
    local_channels = short_filter.shape[2]
    group_width = local_channels // local_groups
    groups = width // group_width
    n_docs = doc_lengths.shape[0]

    sizes = (short_filter.size, decay_rate.size, residue.size, skip_gain.size)
    flat = jnp.concatenate(
        [short_filter.reshape(-1), decay_rate.reshape(-1), residue.reshape(-1), skip_gain.reshape(-1)]
    )
    every = lax.all_gather(flat, "ch")
    o1 = sizes[0]
    o2 = o1 + sizes[1]
    o3 = o2 + sizes[2]
    sf_all = jnp.transpose(every[:, :o1].reshape(n_ch, 3, 3, local_channels), (1, 2, 0, 3)).reshape(
        3, 3, n_ch * local_channels
    )
    sf = lax.dynamic_slice_in_dim(sf_all, here_ctx * width, width, 2)
    rate = lax.dynamic_slice_in_dim(every[:, o1:o2].reshape(n_ch * local_groups, modes), here_ctx * groups, groups, 0)
    res = lax.dynamic_slice_in_dim(every[:, o2:o3].reshape(n_ch * local_groups, modes), here_ctx * groups, groups, 0)
    skip = lax.dynamic_slice_in_dim(every[:, o3:].reshape(n_ch * local_channels), here_ctx * width, width, 0)
    coefficient = res * jnp.sqrt(1.0 - jnp.exp(-2.0 * rate))

    sending = jnp.transpose(projections.reshape(feeds, rows_here, n_ctx, width), (2, 1, 0, 3))
    sending = sending.reshape(n_ctx, rows_here, feeds * width)
    received = lax.all_to_all(sending, "ctx", 0, 0, tiled=True).reshape(n_ctx * rows_here, feeds * width)
    routing = attention_order.reshape(n_ctx, tokens // n_ctx)
    mine = lax.dynamic_slice_in_dim(routing, here_ch * rows_here, rows_here, 1).reshape(n_ctx * rows_here)
    placer = (
        (mine - here_ch * span)[None, :] == jnp.arange(span, dtype=jnp.int32)[:, None]
    ).astype(jnp.bfloat16)
    ordered = jnp.dot(placer, received, preferred_element_type=jnp.float32).astype(jnp.bfloat16)

    earlier = lax.ppermute(ordered[span - 2 :, :], "ch", [(i, i + 1) for i in range(n_ch - 1)])
    widened = jnp.concatenate([earlier, ordered], axis=0).astype(jnp.float32)
    widened = jnp.stack([widened[:, p * width : (p + 1) * width] for p in range(feeds)])
    bounds = jnp.cumsum(doc_lengths).astype(jnp.int32)
    span_docs = doc_index(here_ch * span - 2 + jnp.arange(span + 2, dtype=jnp.int32), bounds)
    current = span_docs[2:]
    keep_one = (span_docs[1 : 1 + span] == current).astype(jnp.float32)[None, :, None]
    keep_two = (span_docs[0:span] == current).astype(jnp.float32)[None, :, None]
    featured = (
        sf[:, 0, None, :] * widened[:, 2:]
        + sf[:, 1, None, :] * widened[:, 1 : 1 + span] * keep_one
        + sf[:, 2, None, :] * widened[:, 0:span] * keep_two
    )
    gated = (featured[1] * featured[2]).astype(jnp.bfloat16)

    steps = jnp.arange(block, dtype=jnp.float32)
    falling = coefficient[:, None, :] * jnp.exp(-rate[:, None, :] * steps[None, :, None])
    rising = jnp.exp(rate[:, :, None] * steps[None, None, :])
    lower = steps[:, None] >= steps[None, :]
    toeplitz = jnp.where(
        lower[None], jnp.einsum("gtm,gms->gts", falling, rising, precision=highest), 0.0
    )
    toe_hi = toeplitz.astype(jnp.bfloat16)
    toe_lo = (toeplitz - toe_hi.astype(jnp.float32)).astype(jnp.bfloat16)
    toe_both = jnp.concatenate([toe_hi, toe_lo], axis=2)
    x = gated.reshape(chunks, block, groups, group_width)
    docs_k = current.reshape(chunks, block)
    doc_ids = jnp.arange(n_docs, dtype=jnp.int32)
    in_doc = docs_k[None] == doc_ids[:, None, None]
    xd = jnp.where(in_doc[:, :, :, None, None], x[None], jnp.zeros((), jnp.bfloat16))
    xd = jnp.concatenate([xd, xd], axis=2)
    per_doc = jnp.einsum("gts,dksgc->dktgc", toe_both, xd, preferred_element_type=jnp.float32)
    intra = jnp.sum(jnp.where(in_doc[:, :, :, None, None], per_doc, 0.0), axis=0)

    x32 = x.astype(jnp.float32)
    ends_doc = docs_k[:, block - 1]
    at_end = (docs_k == ends_doc[:, None]).astype(jnp.float32)
    towards_end = jnp.exp(-rate[:, :, None] * (block - 1.0 - steps)[None, None, :])
    chunk_state = jnp.einsum(
        "gms,ksgc->kgmc", towards_end, x32 * at_end[:, :, None, None], precision=highest
    )
    chunk_ids = jnp.arange(chunks, dtype=jnp.int32)
    lag = (chunk_ids[:, None] - chunk_ids[None, :]).astype(jnp.float32)
    linked = (chunk_ids[:, None] >= chunk_ids[None, :]) & (ends_doc[:, None] == ends_doc[None, :])
    carry_weight = jnp.where(
        linked[:, :, None, None],
        jnp.exp(-rate[None, None] * (block * jnp.maximum(lag, 0.0))[:, :, None, None]),
        0.0,
    )
    local_state = jnp.sum(carry_weight[:, :, :, :, None] * chunk_state[None], axis=1)

    previous_doc = span_docs[1]
    span_factor = jnp.exp(-rate * float(span)) * (previous_doc == current[span - 1]).astype(jnp.float32)
    packed = jnp.concatenate([span_factor.reshape(-1), local_state[chunks - 1].reshape(-1)])
    gathered = lax.all_gather(packed, "ch")
    factors = gathered[:, : groups * modes].reshape(n_ch, groups, modes, 1)
    states = gathered[:, groups * modes :].reshape(n_ch, groups, modes, group_width)
    entering = jnp.zeros((groups, modes, group_width), jnp.float32)
    for source in range(n_ch):
        entering = jnp.where(source < here_ch, factors[source] * entering + states[source], entering)

    reach = jnp.exp(-rate[None] * (block * (chunk_ids + 1.0))[:, None, None])
    joined = (previous_doc == ends_doc).astype(jnp.float32)[:, None, None, None]
    total_state = local_state + reach[..., None] * joined * entering[None]
    before = jnp.concatenate([entering[None], total_state[: chunks - 1]], axis=0)
    start_prev_doc = jnp.concatenate([previous_doc[None], docs_k[: chunks - 1, block - 1]])
    from_before = (docs_k == start_prev_doc[:, None]).astype(jnp.float32)
    decaying = coefficient[:, None, :] * jnp.exp(-rate[:, None, :] * (steps + 1.0)[None, :, None])
    incoming = jnp.einsum("gtm,kgmc->ktgc", decaying, before, precision=highest)
    filtered = intra + incoming * from_before[:, :, None, None]

    gated32 = gated.astype(jnp.float32)
    combined = filtered.reshape(span, width) + skip[None, :] * gated32
    mixed = (featured[0] * combined).astype(jnp.bfloat16)

    back = jnp.dot(placer.T, mixed, preferred_element_type=jnp.float32).astype(jnp.bfloat16)
    returned = lax.all_to_all(back.reshape(n_ctx, rows_here, width), "ctx", 0, 0, tiled=True)
    return jnp.transpose(returned, (1, 0, 2)).reshape(rows_here, n_ctx * width)


def solution(mesh):
    placed = (
        P(None, ("ctx", "ch"), None),
        P(),
        P(),
        P(None, None, "ch"),
        P("ch", None),
        P("ch", None),
        P("ch"),
    )
    return jax.shard_map(
        shards, mesh=mesh, in_specs=placed, out_specs=P(("ctx", "ch"), None), check_vma=False
    )
```

```python
import jax
import jax.numpy as jnp
from jax import lax
from jax.sharding import PartitionSpec as P

highest = lax.Precision.HIGHEST


def doc_index(positions, bounds):
    found = jnp.sum((positions[:, None] >= bounds[None, :]).astype(jnp.int32), axis=1)
    return jnp.where(positions >= 0, found, -1)


def shards(projections, attention_order, doc_lengths, short_filter, decay_rate, residue, skip_gain):
    n_ctx = lax.axis_size("ctx")
    n_ch = lax.axis_size("ch")
    here_ctx = lax.axis_index("ctx")
    here_ch = lax.axis_index("ch")
    feeds, rows_here, channels = projections.shape
    tokens = attention_order.shape[0]
    block = tokens // n_ctx
    slot = block // n_ctx
    chunks = rows_here // slot
    span = chunks * block
    width = channels // n_ctx
    local_groups, modes = decay_rate.shape
    local_channels = short_filter.shape[2]
    group_width = local_channels // local_groups
    groups = width // group_width
    n_docs = doc_lengths.shape[0]

    sizes = (short_filter.size, decay_rate.size, residue.size, skip_gain.size)
    flat = jnp.concatenate(
        [short_filter.reshape(-1), decay_rate.reshape(-1), residue.reshape(-1), skip_gain.reshape(-1)]
    )
    every = lax.all_gather(flat, "ch")
    o1 = sizes[0]
    o2 = o1 + sizes[1]
    o3 = o2 + sizes[2]
    sf_all = jnp.transpose(every[:, :o1].reshape(n_ch, 3, 3, local_channels), (1, 2, 0, 3)).reshape(
        3, 3, n_ch * local_channels
    )
    sf = lax.dynamic_slice_in_dim(sf_all, here_ctx * width, width, 2)
    rate = lax.dynamic_slice_in_dim(every[:, o1:o2].reshape(n_ch * local_groups, modes), here_ctx * groups, groups, 0)
    res = lax.dynamic_slice_in_dim(every[:, o2:o3].reshape(n_ch * local_groups, modes), here_ctx * groups, groups, 0)
    skip = lax.dynamic_slice_in_dim(every[:, o3:].reshape(n_ch * local_channels), here_ctx * width, width, 0)
    coefficient = res * jnp.sqrt(1.0 - jnp.exp(-2.0 * rate))

    sending = jnp.transpose(projections.reshape(feeds, rows_here, n_ctx, width), (2, 1, 0, 3))
    sending = sending.reshape(n_ctx, rows_here, feeds * width)
    received = lax.all_to_all(sending, "ctx", 0, 0, tiled=True).reshape(n_ctx * rows_here, feeds * width)
    routing = attention_order.reshape(n_ctx, tokens // n_ctx)
    mine = lax.dynamic_slice_in_dim(routing, here_ch * rows_here, rows_here, 1).reshape(n_ctx * rows_here)
    placer = (
        (mine - here_ch * span)[None, :] == jnp.arange(span, dtype=jnp.int32)[:, None]
    ).astype(jnp.bfloat16)
    ordered = jnp.dot(placer, received, preferred_element_type=jnp.float32).astype(jnp.bfloat16)

    earlier = lax.ppermute(ordered[span - 2 :, :], "ch", [(i, i + 1) for i in range(n_ch - 1)])
    widened = jnp.concatenate([earlier, ordered], axis=0).astype(jnp.float32)
    widened = jnp.stack([widened[:, p * width : (p + 1) * width] for p in range(feeds)])
    bounds = jnp.cumsum(doc_lengths).astype(jnp.int32)
    span_docs = doc_index(here_ch * span - 2 + jnp.arange(span + 2, dtype=jnp.int32), bounds)
    current = span_docs[2:]
    keep_one = (span_docs[1 : 1 + span] == current).astype(jnp.float32)[None, :, None]
    keep_two = (span_docs[0:span] == current).astype(jnp.float32)[None, :, None]
    featured = (
        sf[:, 0, None, :] * widened[:, 2:]
        + sf[:, 1, None, :] * widened[:, 1 : 1 + span] * keep_one
        + sf[:, 2, None, :] * widened[:, 0:span] * keep_two
    )
    gated = (featured[1] * featured[2]).astype(jnp.bfloat16)

    steps = jnp.arange(block, dtype=jnp.float32)
    falling = coefficient[:, None, :] * jnp.exp(-rate[:, None, :] * steps[None, :, None])
    rising = jnp.exp(rate[:, :, None] * steps[None, None, :])
    lower = steps[:, None] >= steps[None, :]
    toeplitz = jnp.where(
        lower[None], jnp.einsum("gtm,gms->gts", falling, rising, precision=highest), 0.0
    )
    toe_hi = toeplitz.astype(jnp.bfloat16)
    toe_lo = (toeplitz - toe_hi.astype(jnp.float32)).astype(jnp.bfloat16)
    toe_both = jnp.concatenate([toe_hi, toe_lo], axis=2)
    x = gated.reshape(chunks, block, groups, group_width)
    docs_k = current.reshape(chunks, block)
    doc_ids = jnp.arange(n_docs, dtype=jnp.int32)
    in_doc = docs_k[None] == doc_ids[:, None, None]
    xd = jnp.where(in_doc[:, :, :, None, None], x[None], jnp.zeros((), jnp.bfloat16))
    xd = jnp.concatenate([xd, xd], axis=2)
    per_doc = jnp.einsum("gts,dksgc->dktgc", toe_both, xd, preferred_element_type=jnp.float32)
    intra = jnp.sum(jnp.where(in_doc[:, :, :, None, None], per_doc, 0.0), axis=0)

    x32 = x.astype(jnp.float32)
    ends_doc = docs_k[:, block - 1]
    at_end = (docs_k == ends_doc[:, None]).astype(jnp.float32)
    towards_end = jnp.exp(-rate[:, :, None] * (block - 1.0 - steps)[None, None, :])
    chunk_state = jnp.einsum(
        "gms,ksgc->kgmc", towards_end, x32 * at_end[:, :, None, None], precision=highest
    )
    chunk_ids = jnp.arange(chunks, dtype=jnp.int32)
    lag = (chunk_ids[:, None] - chunk_ids[None, :]).astype(jnp.float32)
    linked = (chunk_ids[:, None] >= chunk_ids[None, :]) & (ends_doc[:, None] == ends_doc[None, :])
    carry_weight = jnp.where(
        linked[:, :, None, None],
        jnp.exp(-rate[None, None] * (block * jnp.maximum(lag, 0.0))[:, :, None, None]),
        0.0,
    )
    local_state = jnp.sum(carry_weight[:, :, :, :, None] * chunk_state[None], axis=1)

    previous_doc = span_docs[1]
    gathered = lax.all_gather(local_state[chunks - 1], "ch")
    span_ids = jnp.arange(n_ch, dtype=jnp.int32)
    span_end_doc = doc_index((span_ids + 1) * span - 1, bounds)
    distance = jnp.maximum(here_ch - 1 - span_ids, 0).astype(jnp.float32)
    counted = (span_ids < here_ch) & (span_end_doc == previous_doc)
    span_weight = jnp.where(
        counted[:, None, None], jnp.exp(-rate[None] * (float(span) * distance)[:, None, None]), 0.0
    )
    entering = jnp.sum(span_weight[..., None] * gathered, axis=0)

    reach = jnp.exp(-rate[None] * (block * (chunk_ids + 1.0))[:, None, None])
    joined = (previous_doc == ends_doc).astype(jnp.float32)[:, None, None, None]
    total_state = local_state + reach[..., None] * joined * entering[None]
    before = jnp.concatenate([entering[None], total_state[: chunks - 1]], axis=0)
    start_prev_doc = jnp.concatenate([previous_doc[None], docs_k[: chunks - 1, block - 1]])
    from_before = (docs_k == start_prev_doc[:, None]).astype(jnp.float32)
    decaying = coefficient[:, None, :] * jnp.exp(-rate[:, None, :] * (steps + 1.0)[None, :, None])
    incoming = jnp.einsum("gtm,kgmc->ktgc", decaying, before, precision=highest)
    filtered = intra + incoming * from_before[:, :, None, None]

    gated32 = gated.astype(jnp.float32)
    combined = filtered.reshape(span, width) + skip[None, :] * gated32
    mixed = (featured[0] * combined).astype(jnp.bfloat16)

    back = jnp.dot(placer.T, mixed, preferred_element_type=jnp.float32).astype(jnp.bfloat16)
    returned = lax.all_to_all(back.reshape(n_ctx, rows_here, width), "ctx", 0, 0, tiled=True)
    return jnp.transpose(returned, (1, 0, 2)).reshape(rows_here, n_ctx * width)


def solution(mesh):
    placed = (
        P(None, ("ctx", "ch"), None),
        P(),
        P(),
        P(None, None, "ch"),
        P("ch", None),
        P("ch", None),
        P("ch"),
    )
    return jax.shard_map(
        shards, mesh=mesh, in_specs=placed, out_specs=P(("ctx", "ch"), None), check_vma=False
    )
```

```python
import jax
import jax.numpy as jnp
from jax import lax
from jax.sharding import PartitionSpec as P

highest = lax.Precision.HIGHEST


def doc_index(positions, bounds):
    found = jnp.sum((positions[:, None] >= bounds[None, :]).astype(jnp.int32), axis=1)
    return jnp.where(positions >= 0, found, -1)


def shards(projections, attention_order, doc_lengths, short_filter, decay_rate, residue, skip_gain):
    n_ctx = lax.axis_size("ctx")
    n_ch = lax.axis_size("ch")
    here_ctx = lax.axis_index("ctx")
    here_ch = lax.axis_index("ch")
    feeds, rows_here, channels = projections.shape
    tokens = attention_order.shape[0]
    block = tokens // n_ctx
    slot = block // n_ctx
    chunks = rows_here // slot
    span = chunks * block
    width = channels // n_ctx
    local_groups, modes = decay_rate.shape
    local_channels = short_filter.shape[2]
    group_width = local_channels // local_groups
    groups = width // group_width
    n_docs = doc_lengths.shape[0]

    sizes = (short_filter.size, decay_rate.size, residue.size, skip_gain.size)
    flat = jnp.concatenate(
        [short_filter.reshape(-1), decay_rate.reshape(-1), residue.reshape(-1), skip_gain.reshape(-1)]
    )
    every = lax.all_gather(flat, "ch")
    o1 = sizes[0]
    o2 = o1 + sizes[1]
    o3 = o2 + sizes[2]
    sf_all = jnp.transpose(every[:, :o1].reshape(n_ch, 3, 3, local_channels), (1, 2, 0, 3)).reshape(
        3, 3, n_ch * local_channels
    )
    sf = lax.dynamic_slice_in_dim(sf_all, here_ctx * width, width, 2)
    rate = lax.dynamic_slice_in_dim(every[:, o1:o2].reshape(n_ch * local_groups, modes), here_ctx * groups, groups, 0)
    res = lax.dynamic_slice_in_dim(every[:, o2:o3].reshape(n_ch * local_groups, modes), here_ctx * groups, groups, 0)
    skip = lax.dynamic_slice_in_dim(every[:, o3:].reshape(n_ch * local_channels), here_ctx * width, width, 0)
    coefficient = res * jnp.sqrt(1.0 - jnp.exp(-2.0 * rate))

    routing = attention_order.reshape(n_ctx, tokens // n_ctx)
    mine = lax.dynamic_slice_in_dim(routing, here_ch * rows_here, rows_here, 1).reshape(n_ctx * rows_here)
    placer = (
        (mine - here_ch * span)[None, :] == jnp.arange(span, dtype=jnp.int32)[:, None]
    ).astype(jnp.bfloat16)

    arrived = []

    def arrive(part):
        count = part.shape[0]
        sending = jnp.transpose(part.reshape(count, rows_here, n_ctx, width), (2, 1, 0, 3))
        sending = sending.reshape(n_ctx, rows_here, count * width)
        received = lax.all_to_all(sending, "ctx", 0, 0, tiled=True).reshape(n_ctx * rows_here, count * width)
        arrived.append(received)
        ordered = jnp.dot(placer, received, preferred_element_type=jnp.float32).astype(jnp.bfloat16)
        earlier = lax.ppermute(ordered[span - 2 :, :], "ch", [(i, i + 1) for i in range(n_ch - 1)])
        widened = jnp.concatenate([earlier, ordered], axis=0).astype(jnp.float32)
        return [widened[:, p * width : (p + 1) * width] for p in range(count)]

    bounds = jnp.cumsum(doc_lengths).astype(jnp.int32)
    span_docs = doc_index(here_ch * span - 2 + jnp.arange(span + 2, dtype=jnp.int32), bounds)
    current = span_docs[2:]
    keep_one = (span_docs[1 : 1 + span] == current).astype(jnp.float32)[:, None]
    keep_two = (span_docs[0:span] == current).astype(jnp.float32)[:, None]

    def feature(p, rows):
        return (
            sf[p, 0, None, :] * rows[2:]
            + sf[p, 1, None, :] * rows[1 : 1 + span] * keep_one
            + sf[p, 2, None, :] * rows[0:span] * keep_two
        )

    key_rows, value_rows = arrive(projections[1:3])
    featured_key = feature(1, key_rows)
    featured_value = feature(2, value_rows)
    gated = (featured_key * featured_value).astype(jnp.bfloat16)

    steps = jnp.arange(block, dtype=jnp.float32)
    falling = coefficient[:, None, :] * jnp.exp(-rate[:, None, :] * steps[None, :, None])
    rising = jnp.exp(rate[:, :, None] * steps[None, None, :])
    lower = steps[:, None] >= steps[None, :]
    toeplitz = jnp.where(
        lower[None], jnp.einsum("gtm,gms->gts", falling, rising, precision=highest), 0.0
    )
    toe_hi = toeplitz.astype(jnp.bfloat16)
    toe_lo = (toeplitz - toe_hi.astype(jnp.float32)).astype(jnp.bfloat16)
    toe_both = jnp.concatenate([toe_hi, toe_lo], axis=2)
    x = gated.reshape(chunks, block, groups, group_width)
    docs_k = current.reshape(chunks, block)
    doc_ids = jnp.arange(n_docs, dtype=jnp.int32)
    in_doc = docs_k[None] == doc_ids[:, None, None]
    xd = jnp.where(in_doc[:, :, :, None, None], x[None], jnp.zeros((), jnp.bfloat16))
    xd = jnp.concatenate([xd, xd], axis=2)
    per_doc = jnp.einsum("gts,dksgc->dktgc", toe_both, xd, preferred_element_type=jnp.float32)
    intra = jnp.sum(jnp.where(in_doc[:, :, :, None, None], per_doc, 0.0), axis=0)

    x32 = x.astype(jnp.float32)
    ends_doc = docs_k[:, block - 1]
    at_end = (docs_k == ends_doc[:, None]).astype(jnp.float32)
    towards_end = jnp.exp(-rate[:, :, None] * (block - 1.0 - steps)[None, None, :])
    chunk_state = jnp.einsum(
        "gms,ksgc->kgmc", towards_end, x32 * at_end[:, :, None, None], precision=highest
    )
    chunk_ids = jnp.arange(chunks, dtype=jnp.int32)
    lag = (chunk_ids[:, None] - chunk_ids[None, :]).astype(jnp.float32)
    linked = (chunk_ids[:, None] >= chunk_ids[None, :]) & (ends_doc[:, None] == ends_doc[None, :])
    carry_weight = jnp.where(
        linked[:, :, None, None],
        jnp.exp(-rate[None, None] * (block * jnp.maximum(lag, 0.0))[:, :, None, None]),
        0.0,
    )
    local_state = jnp.sum(carry_weight[:, :, :, :, None] * chunk_state[None], axis=1)

    previous_doc = span_docs[1]
    gathered = lax.all_gather(local_state[chunks - 1], "ch")
    span_ids = jnp.arange(n_ch, dtype=jnp.int32)
    span_end_doc = doc_index((span_ids + 1) * span - 1, bounds)
    distance = jnp.maximum(here_ch - 1 - span_ids, 0).astype(jnp.float32)
    counted = (span_ids < here_ch) & (span_end_doc == previous_doc)
    span_weight = jnp.where(
        counted[:, None, None], jnp.exp(-rate[None] * (float(span) * distance)[:, None, None]), 0.0
    )
    entering = jnp.sum(span_weight[..., None] * gathered, axis=0)

    reach = jnp.exp(-rate[None] * (block * (chunk_ids + 1.0))[:, None, None])
    joined = (previous_doc == ends_doc).astype(jnp.float32)[:, None, None, None]
    total_state = local_state + reach[..., None] * joined * entering[None]
    before = jnp.concatenate([entering[None], total_state[: chunks - 1]], axis=0)
    start_prev_doc = jnp.concatenate([previous_doc[None], docs_k[: chunks - 1, block - 1]])
    from_before = (docs_k == start_prev_doc[:, None]).astype(jnp.float32)
    decaying = coefficient[:, None, :] * jnp.exp(-rate[:, None, :] * (steps + 1.0)[None, :, None])
    incoming = jnp.einsum("gtm,kgmc->ktgc", decaying, before, precision=highest)
    filtered = intra + incoming * from_before[:, :, None, None]

    gated32 = gated.astype(jnp.float32)
    combined = filtered.reshape(span, width) + skip[None, :] * gated32
    _, query_part = lax.optimization_barrier((arrived[0], projections[0:1]))
    (query_rows,) = arrive(query_part)
    mixed = (feature(0, query_rows) * combined).astype(jnp.bfloat16)

    back = jnp.dot(placer.T, mixed, preferred_element_type=jnp.float32).astype(jnp.bfloat16)
    returned = lax.all_to_all(back.reshape(n_ctx, rows_here, width), "ctx", 0, 0, tiled=True)
    return jnp.transpose(returned, (1, 0, 2)).reshape(rows_here, n_ctx * width)


def solution(mesh):
    placed = (
        P(None, ("ctx", "ch"), None),
        P(),
        P(),
        P(None, None, "ch"),
        P("ch", None),
        P("ch", None),
        P("ch"),
    )
    return jax.shard_map(
        shards, mesh=mesh, in_specs=placed, out_specs=P(("ctx", "ch"), None), check_vma=False
    )
```

```python
import jax
import jax.numpy as jnp
from jax import lax
from jax.sharding import PartitionSpec as P

highest = lax.Precision.HIGHEST


def doc_index(positions, bounds):
    found = jnp.sum((positions[:, None] >= bounds[None, :]).astype(jnp.int32), axis=1)
    return jnp.where(positions >= 0, found, -1)


def ctx_exchange(value):
    n_z, n_x = lax.axis_size("cz"), lax.axis_size("cx")
    rest = value.shape[1:]
    value = value.reshape((n_z, n_x) + rest)
    value = lax.all_to_all(value, "cx", 1, 1, tiled=True)
    value = lax.all_to_all(value, "cz", 0, 0, tiled=True)
    return value.reshape((n_z * n_x,) + rest)


def shards(projections, attention_order, doc_lengths, short_filter, decay_rate, residue, skip_gain):
    n_ctx = lax.axis_size("cz") * lax.axis_size("cx")
    n_ch = lax.axis_size("ch")
    here_ctx = lax.axis_index("cz") * lax.axis_size("cx") + lax.axis_index("cx")
    here_ch = lax.axis_index("ch")
    feeds, rows_here, channels = projections.shape
    tokens = attention_order.shape[0]
    block = tokens // n_ctx
    slot = block // n_ctx
    chunks = rows_here // slot
    span = chunks * block
    width = channels // n_ctx
    local_groups, modes = decay_rate.shape
    local_channels = short_filter.shape[2]
    group_width = local_channels // local_groups
    groups = width // group_width
    n_docs = doc_lengths.shape[0]

    sizes = (short_filter.size, decay_rate.size, residue.size, skip_gain.size)
    flat = jnp.concatenate(
        [short_filter.reshape(-1), decay_rate.reshape(-1), residue.reshape(-1), skip_gain.reshape(-1)]
    )
    every = lax.all_gather(flat, "ch")
    o1 = sizes[0]
    o2 = o1 + sizes[1]
    o3 = o2 + sizes[2]
    sf_all = jnp.transpose(every[:, :o1].reshape(n_ch, 3, 3, local_channels), (1, 2, 0, 3)).reshape(
        3, 3, n_ch * local_channels
    )
    sf = lax.dynamic_slice_in_dim(sf_all, here_ctx * width, width, 2)
    rate = lax.dynamic_slice_in_dim(every[:, o1:o2].reshape(n_ch * local_groups, modes), here_ctx * groups, groups, 0)
    res = lax.dynamic_slice_in_dim(every[:, o2:o3].reshape(n_ch * local_groups, modes), here_ctx * groups, groups, 0)
    skip = lax.dynamic_slice_in_dim(every[:, o3:].reshape(n_ch * local_channels), here_ctx * width, width, 0)
    coefficient = res * jnp.sqrt(1.0 - jnp.exp(-2.0 * rate))

    routing = attention_order.reshape(n_ctx, tokens // n_ctx)
    mine = lax.dynamic_slice_in_dim(routing, here_ch * rows_here, rows_here, 1).reshape(n_ctx * rows_here)
    placer = (
        (mine - here_ch * span)[None, :] == jnp.arange(span, dtype=jnp.int32)[:, None]
    ).astype(jnp.bfloat16)

    arrived = []

    def arrive(part):
        count = part.shape[0]
        sending = jnp.transpose(part.reshape(count, rows_here, n_ctx, width), (2, 1, 0, 3))
        sending = sending.reshape(n_ctx, rows_here, count * width)
        received = ctx_exchange(sending).reshape(n_ctx * rows_here, count * width)
        arrived.append(received)
        ordered = jnp.dot(placer, received, preferred_element_type=jnp.float32).astype(jnp.bfloat16)
        earlier = lax.ppermute(ordered[span - 2 :, :], "ch", [(i, i + 1) for i in range(n_ch - 1)])
        widened = jnp.concatenate([earlier, ordered], axis=0).astype(jnp.float32)
        return [widened[:, p * width : (p + 1) * width] for p in range(count)]

    bounds = jnp.cumsum(doc_lengths).astype(jnp.int32)
    span_docs = doc_index(here_ch * span - 2 + jnp.arange(span + 2, dtype=jnp.int32), bounds)
    current = span_docs[2:]
    keep_one = (span_docs[1 : 1 + span] == current).astype(jnp.float32)[:, None]
    keep_two = (span_docs[0:span] == current).astype(jnp.float32)[:, None]

    def feature(p, rows):
        return (
            sf[p, 0, None, :] * rows[2:]
            + sf[p, 1, None, :] * rows[1 : 1 + span] * keep_one
            + sf[p, 2, None, :] * rows[0:span] * keep_two
        )

    key_rows, value_rows = arrive(projections[1:3])
    featured_key = feature(1, key_rows)
    featured_value = feature(2, value_rows)
    gated = (featured_key * featured_value).astype(jnp.bfloat16)

    steps = jnp.arange(block, dtype=jnp.float32)
    falling = coefficient[:, None, :] * jnp.exp(-rate[:, None, :] * steps[None, :, None])
    rising = jnp.exp(rate[:, :, None] * steps[None, None, :])
    lower = steps[:, None] >= steps[None, :]
    toeplitz = jnp.where(
        lower[None], jnp.einsum("gtm,gms->gts", falling, rising, precision=highest), 0.0
    )
    toe_hi = toeplitz.astype(jnp.bfloat16)
    toe_lo = (toeplitz - toe_hi.astype(jnp.float32)).astype(jnp.bfloat16)
    toe_both = jnp.concatenate([toe_hi, toe_lo], axis=2)
    x = gated.reshape(chunks, block, groups, group_width)
    docs_k = current.reshape(chunks, block)
    doc_ids = jnp.arange(n_docs, dtype=jnp.int32)
    in_doc = docs_k[None] == doc_ids[:, None, None]
    xd = jnp.where(in_doc[:, :, :, None, None], x[None], jnp.zeros((), jnp.bfloat16))
    xd = jnp.concatenate([xd, xd], axis=2)
    per_doc = jnp.einsum("gts,dksgc->dktgc", toe_both, xd, preferred_element_type=jnp.float32)
    intra = jnp.sum(jnp.where(in_doc[:, :, :, None, None], per_doc, 0.0), axis=0)

    x32 = x.astype(jnp.float32)
    ends_doc = docs_k[:, block - 1]
    at_end = (docs_k == ends_doc[:, None]).astype(jnp.float32)
    towards_end = jnp.exp(-rate[:, :, None] * (block - 1.0 - steps)[None, None, :])
    chunk_state = jnp.einsum(
        "gms,ksgc->kgmc", towards_end, x32 * at_end[:, :, None, None], precision=highest
    )
    chunk_ids = jnp.arange(chunks, dtype=jnp.int32)
    lag = (chunk_ids[:, None] - chunk_ids[None, :]).astype(jnp.float32)
    linked = (chunk_ids[:, None] >= chunk_ids[None, :]) & (ends_doc[:, None] == ends_doc[None, :])
    carry_weight = jnp.where(
        linked[:, :, None, None],
        jnp.exp(-rate[None, None] * (block * jnp.maximum(lag, 0.0))[:, :, None, None]),
        0.0,
    )
    local_state = jnp.sum(carry_weight[:, :, :, :, None] * chunk_state[None], axis=1)

    previous_doc = span_docs[1]
    gathered = lax.all_gather(local_state[chunks - 1], "ch")
    span_ids = jnp.arange(n_ch, dtype=jnp.int32)
    span_end_doc = doc_index((span_ids + 1) * span - 1, bounds)
    distance = jnp.maximum(here_ch - 1 - span_ids, 0).astype(jnp.float32)
    counted = (span_ids < here_ch) & (span_end_doc == previous_doc)
    span_weight = jnp.where(
        counted[:, None, None], jnp.exp(-rate[None] * (float(span) * distance)[:, None, None]), 0.0
    )
    entering = jnp.sum(span_weight[..., None] * gathered, axis=0)

    reach = jnp.exp(-rate[None] * (block * (chunk_ids + 1.0))[:, None, None])
    joined = (previous_doc == ends_doc).astype(jnp.float32)[:, None, None, None]
    total_state = local_state + reach[..., None] * joined * entering[None]
    before = jnp.concatenate([entering[None], total_state[: chunks - 1]], axis=0)
    start_prev_doc = jnp.concatenate([previous_doc[None], docs_k[: chunks - 1, block - 1]])
    from_before = (docs_k == start_prev_doc[:, None]).astype(jnp.float32)
    decaying = coefficient[:, None, :] * jnp.exp(-rate[:, None, :] * (steps + 1.0)[None, :, None])
    incoming = jnp.einsum("gtm,kgmc->ktgc", decaying, before, precision=highest)
    filtered = intra + incoming * from_before[:, :, None, None]

    gated32 = gated.astype(jnp.float32)
    combined = filtered.reshape(span, width) + skip[None, :] * gated32
    _, query_part = lax.optimization_barrier((arrived[0], projections[0:1]))
    (query_rows,) = arrive(query_part)
    mixed = (feature(0, query_rows) * combined).astype(jnp.bfloat16)

    back = jnp.dot(placer.T, mixed, preferred_element_type=jnp.float32).astype(jnp.bfloat16)
    returned = ctx_exchange(back.reshape(n_ctx, rows_here, width))
    return jnp.transpose(returned, (1, 0, 2)).reshape(rows_here, n_ctx * width)


def solution(mesh):
    n_ctx, n_ch = mesh.devices.shape
    n_x = 4 if n_ctx % 4 == 0 else 1
    split = jax.sharding.Mesh(mesh.devices.reshape(n_ctx // n_x, n_x, n_ch), ("cz", "cx", "ch"))
    rows = ("cz", "cx", "ch")
    placed = (
        P(None, rows, None),
        P(),
        P(),
        P(None, None, "ch"),
        P("ch", None),
        P("ch", None),
        P("ch"),
    )
    return jax.shard_map(shards, mesh=split, in_specs=placed, out_specs=P(rows, None), check_vma=False)
```

```python
import jax
import jax.numpy as jnp
from jax import lax
from jax.sharding import PartitionSpec as P

highest = lax.Precision.HIGHEST


def doc_index(positions, bounds):
    found = jnp.sum((positions[:, None] >= bounds[None, :]).astype(jnp.int32), axis=1)
    return jnp.where(positions >= 0, found, -1)


def shards(projections, attention_order, doc_lengths, short_filter, decay_rate, residue, skip_gain):
    n_ctx = lax.axis_size("ctx")
    n_ch = lax.axis_size("ch")
    here_ctx = lax.axis_index("ctx")
    here_ch = lax.axis_index("ch")
    feeds, rows_here, channels = projections.shape
    tokens = attention_order.shape[0]
    block = tokens // n_ctx
    slot = block // n_ctx
    chunks = rows_here // slot
    span = chunks * block
    width = channels // n_ctx
    local_groups, modes = decay_rate.shape
    local_channels = short_filter.shape[2]
    group_width = local_channels // local_groups
    groups = width // group_width
    n_docs = doc_lengths.shape[0]

    sizes = (short_filter.size, decay_rate.size, residue.size, skip_gain.size)
    flat = jnp.concatenate(
        [short_filter.reshape(-1), decay_rate.reshape(-1), residue.reshape(-1), skip_gain.reshape(-1)]
    )
    every = lax.all_gather(flat, "ch")
    o1 = sizes[0]
    o2 = o1 + sizes[1]
    o3 = o2 + sizes[2]
    sf_all = jnp.transpose(every[:, :o1].reshape(n_ch, 3, 3, local_channels), (1, 2, 0, 3)).reshape(
        3, 3, n_ch * local_channels
    )
    sf = lax.dynamic_slice_in_dim(sf_all, here_ctx * width, width, 2)
    rate = lax.dynamic_slice_in_dim(every[:, o1:o2].reshape(n_ch * local_groups, modes), here_ctx * groups, groups, 0)
    res = lax.dynamic_slice_in_dim(every[:, o2:o3].reshape(n_ch * local_groups, modes), here_ctx * groups, groups, 0)
    skip = lax.dynamic_slice_in_dim(every[:, o3:].reshape(n_ch * local_channels), here_ctx * width, width, 0)
    coefficient = res * jnp.sqrt(1.0 - jnp.exp(-2.0 * rate))

    routing = attention_order.reshape(n_ctx, tokens // n_ctx)
    mine = lax.dynamic_slice_in_dim(routing, here_ch * rows_here, rows_here, 1).reshape(n_ctx * rows_here)
    placer = (
        (mine - here_ch * span)[None, :] == jnp.arange(span, dtype=jnp.int32)[:, None]
    ).astype(jnp.bfloat16)

    arrived = []

    def arrive(part):
        count = part.shape[0]
        sending = jnp.transpose(part.reshape(count, rows_here, n_ctx, width), (2, 1, 0, 3))
        sending = sending.reshape(n_ctx, rows_here, count * width)
        received = lax.all_to_all(sending, "ctx", 0, 0, tiled=True).reshape(n_ctx * rows_here, count * width)
        arrived.append(received)
        ordered = jnp.dot(placer, received, preferred_element_type=jnp.float32).astype(jnp.bfloat16)
        earlier = lax.ppermute(ordered[span - 2 :, :], "ch", [(i, i + 1) for i in range(n_ch - 1)])
        widened = jnp.concatenate([earlier, ordered], axis=0).astype(jnp.float32)
        return [widened[:, p * width : (p + 1) * width] for p in range(count)]

    bounds = jnp.cumsum(doc_lengths).astype(jnp.int32)
    span_docs = doc_index(here_ch * span - 2 + jnp.arange(span + 2, dtype=jnp.int32), bounds)
    current = span_docs[2:]
    keep_one = (span_docs[1 : 1 + span] == current).astype(jnp.float32)[:, None]
    keep_two = (span_docs[0:span] == current).astype(jnp.float32)[:, None]

    def feature(p, rows):
        return (
            sf[p, 0, None, :] * rows[2:]
            + sf[p, 1, None, :] * rows[1 : 1 + span] * keep_one
            + sf[p, 2, None, :] * rows[0:span] * keep_two
        )

    key_rows, value_rows = arrive(projections[1:3])
    featured_key = feature(1, key_rows)
    featured_value = feature(2, value_rows)
    gated = (featured_key * featured_value).astype(jnp.bfloat16)

    steps = jnp.arange(block, dtype=jnp.float32)
    falling = coefficient[:, None, :] * jnp.exp(-rate[:, None, :] * steps[None, :, None])
    rising = jnp.exp(rate[:, :, None] * steps[None, None, :])
    lower = steps[:, None] >= steps[None, :]
    toeplitz = jnp.where(
        lower[None], jnp.einsum("gtm,gms->gts", falling, rising, precision=highest), 0.0
    )
    toe_hi = toeplitz.astype(jnp.bfloat16)
    toe_lo = (toeplitz - toe_hi.astype(jnp.float32)).astype(jnp.bfloat16)
    toe_both = jnp.concatenate([toe_hi, toe_lo], axis=2)
    x = gated.reshape(chunks, block, groups, group_width)
    docs_k = current.reshape(chunks, block)
    doc_ids = jnp.arange(n_docs, dtype=jnp.int32)
    in_doc = docs_k[None] == doc_ids[:, None, None]
    xd = jnp.where(in_doc[:, :, :, None, None], x[None], jnp.zeros((), jnp.bfloat16))
    xd = jnp.concatenate([xd, xd], axis=2)
    per_doc = jnp.einsum("gts,dksgc->dktgc", toe_both, xd, preferred_element_type=jnp.float32)
    intra = jnp.sum(jnp.where(in_doc[:, :, :, None, None], per_doc, 0.0), axis=0)

    x32 = x.astype(jnp.float32)
    ends_doc = docs_k[:, block - 1]
    at_end = (docs_k == ends_doc[:, None]).astype(jnp.float32)
    towards_end = jnp.exp(-rate[:, :, None] * (block - 1.0 - steps)[None, None, :])
    chunk_state = jnp.einsum(
        "gms,ksgc->kgmc", towards_end, x32 * at_end[:, :, None, None], precision=highest
    )
    chunk_ids = jnp.arange(chunks, dtype=jnp.int32)
    lag = (chunk_ids[:, None] - chunk_ids[None, :]).astype(jnp.float32)
    linked = (chunk_ids[:, None] >= chunk_ids[None, :]) & (ends_doc[:, None] == ends_doc[None, :])
    carry_weight = jnp.where(
        linked[:, :, None, None],
        jnp.exp(-rate[None, None] * (block * jnp.maximum(lag, 0.0))[:, :, None, None]),
        0.0,
    )
    local_state = jnp.sum(carry_weight[:, :, :, :, None] * chunk_state[None], axis=1)

    previous_doc = span_docs[1]
    gathered = lax.all_gather(local_state[chunks - 1], "ch")
    span_ids = jnp.arange(n_ch, dtype=jnp.int32)
    span_end_doc = doc_index((span_ids + 1) * span - 1, bounds)
    distance = jnp.maximum(here_ch - 1 - span_ids, 0).astype(jnp.float32)
    counted = (span_ids < here_ch) & (span_end_doc == previous_doc)
    span_weight = jnp.where(
        counted[:, None, None], jnp.exp(-rate[None] * (float(span) * distance)[:, None, None]), 0.0
    )
    entering = jnp.sum(span_weight[..., None] * gathered, axis=0)

    reach = jnp.exp(-rate[None] * (block * (chunk_ids + 1.0))[:, None, None])
    joined = (previous_doc == ends_doc).astype(jnp.float32)[:, None, None, None]
    total_state = local_state + reach[..., None] * joined * entering[None]
    before = jnp.concatenate([entering[None], total_state[: chunks - 1]], axis=0)
    start_prev_doc = jnp.concatenate([previous_doc[None], docs_k[: chunks - 1, block - 1]])
    from_before = (docs_k == start_prev_doc[:, None]).astype(jnp.float32)
    decaying = coefficient[:, None, :] * jnp.exp(-rate[:, None, :] * (steps + 1.0)[None, :, None])
    incoming = jnp.einsum("gtm,kgmc->ktgc", decaying, before, precision=highest)
    filtered = intra + incoming * from_before[:, :, None, None]

    gated32 = gated.astype(jnp.float32)
    combined = filtered.reshape(span, width) + skip[None, :] * gated32
    _, query_part = lax.optimization_barrier((arrived[0], projections[0:1]))
    sending = jnp.transpose(query_part.reshape(1, rows_here, n_ctx, width), (2, 1, 0, 3))
    sending = sending.reshape(n_ctx, rows_here, width)
    received = lax.all_to_all(sending, "ctx", 0, 0, tiled=True).reshape(n_ctx * rows_here, width)
    query = jnp.dot(placer, received, preferred_element_type=jnp.float32).astype(jnp.bfloat16)
    query_halo = lax.ppermute(query[span - 2 :, :], "ch", [(i, i + 1) for i in range(n_ch - 1)])
    query_rows = jnp.concatenate([jnp.zeros((2, width), jnp.bfloat16), query], axis=0).astype(jnp.float32)
    mixed = (feature(0, query_rows) * combined).astype(jnp.bfloat16)
    head = jnp.concatenate([query_halo, query[0:2]], axis=0).astype(jnp.float32)
    head_feature = (
        sf[0, 0, None, :] * head[2:4]
        + sf[0, 1, None, :] * head[1:3] * keep_one[0:2]
        + sf[0, 2, None, :] * head[0:2] * keep_two[0:2]
    )
    head_mixed = (head_feature * combined[0:2]).astype(jnp.bfloat16)

    back = jnp.dot(placer.T, mixed, preferred_element_type=jnp.float32).astype(jnp.bfloat16)
    where_row = (mine - here_ch * span)[:, None]
    back = jnp.where(where_row == 0, head_mixed[0:1], jnp.where(where_row == 1, head_mixed[1:2], back))
    returned = lax.all_to_all(back.reshape(n_ctx, rows_here, width), "ctx", 0, 0, tiled=True)
    return jnp.transpose(returned, (1, 0, 2)).reshape(rows_here, n_ctx * width)


def solution(mesh):
    placed = (
        P(None, ("ctx", "ch"), None),
        P(),
        P(),
        P(None, None, "ch"),
        P("ch", None),
        P("ch", None),
        P("ch"),
    )
    return jax.shard_map(
        shards, mesh=mesh, in_specs=placed, out_specs=P(("ctx", "ch"), None), check_vma=False
    )
```

```python
import jax
import jax.numpy as jnp
from jax import lax
from jax.sharding import PartitionSpec as P


highest = lax.Precision.HIGHEST


def doc_index(positions, bounds):
    found = jnp.sum((positions[:, None] >= bounds[None, :]).astype(jnp.int32), axis=1)
    return jnp.where(positions >= 0, found, -1)


def layer(projections, attention_order, doc_lengths, short_filter, decay_rate, residue, skip_gain):
    n_ctx = lax.axis_size("ctx")
    n_ch = lax.axis_size("ch")
    here_ctx = lax.axis_index("ctx")
    here_ch = lax.axis_index("ch")
    _, rows_here, channels = projections.shape
    tokens = attention_order.shape[0]
    block = tokens // n_ctx
    slot = block // n_ctx
    chunks = rows_here // slot
    span = chunks * block
    width = channels // n_ctx
    local_groups, modes = decay_rate.shape
    local_channels = short_filter.shape[2]
    group_width = local_channels // local_groups
    groups = width // group_width
    n_docs = doc_lengths.shape[0]

    sizes = (short_filter.size, decay_rate.size, residue.size, skip_gain.size)
    flat = jnp.concatenate(
        [short_filter.reshape(-1), decay_rate.reshape(-1), residue.reshape(-1), skip_gain.reshape(-1)]
    )
    every = lax.all_gather(flat, "ch")
    o1 = sizes[0]
    o2 = o1 + sizes[1]
    o3 = o2 + sizes[2]
    sf_all = jnp.transpose(every[:, :o1].reshape(n_ch, 3, 3, local_channels), (1, 2, 0, 3)).reshape(
        3, 3, n_ch * local_channels
    )
    sf = lax.dynamic_slice_in_dim(sf_all, here_ctx * width, width, 2)
    rate = lax.dynamic_slice_in_dim(every[:, o1:o2].reshape(n_ch * local_groups, modes), here_ctx * groups, groups, 0)
    res = lax.dynamic_slice_in_dim(every[:, o2:o3].reshape(n_ch * local_groups, modes), here_ctx * groups, groups, 0)
    skip = lax.dynamic_slice_in_dim(every[:, o3:].reshape(n_ch * local_channels), here_ctx * width, width, 0)
    coefficient = res * jnp.sqrt(1.0 - jnp.exp(-2.0 * rate))

    routing = attention_order.reshape(n_ctx, tokens // n_ctx)
    mine = lax.dynamic_slice_in_dim(routing, here_ch * rows_here, rows_here, 1).reshape(n_ctx * rows_here)
    placer = (
        (mine - here_ch * span)[None, :] == jnp.arange(span, dtype=jnp.int32)[:, None]
    ).astype(jnp.bfloat16)

    arrived = []

    def arrive(part):
        count = part.shape[0]
        sending = jnp.transpose(part.reshape(count, rows_here, n_ctx, width), (2, 1, 0, 3))
        sending = sending.reshape(n_ctx, rows_here, count * width)
        received = lax.all_to_all(sending, "ctx", 0, 0, tiled=True)
        received = received.reshape(n_ctx * rows_here, count * width)
        arrived.append(received)
        ordered = jnp.dot(placer, received, preferred_element_type=jnp.float32).astype(jnp.bfloat16)
        tail = jnp.dot(placer[span - 2 :], received, preferred_element_type=jnp.float32).astype(jnp.bfloat16)
        earlier = lax.ppermute(tail, "ch", [(i, i + 1) for i in range(n_ch - 1)])
        widened = jnp.concatenate([earlier, ordered], axis=0).astype(jnp.float32)
        return [widened[:, p * width : (p + 1) * width] for p in range(count)]

    bounds = jnp.cumsum(doc_lengths).astype(jnp.int32)
    span_docs = doc_index(here_ch * span - 2 + jnp.arange(span + 2, dtype=jnp.int32), bounds)
    current = span_docs[2:]
    keep_one = (span_docs[1 : 1 + span] == current).astype(jnp.float32)[:, None]
    keep_two = (span_docs[0:span] == current).astype(jnp.float32)[:, None]

    def feature(p, rows):
        return (
            sf[p, 0, None, :] * rows[2:]
            + sf[p, 1, None, :] * rows[1 : 1 + span] * keep_one
            + sf[p, 2, None, :] * rows[0:span] * keep_two
        )

    key_rows, value_rows = arrive(projections[1:3])
    featured_key = feature(1, key_rows)
    featured_value = feature(2, value_rows)
    gated = (featured_key * featured_value).astype(jnp.bfloat16)

    steps = jnp.arange(block, dtype=jnp.float32)
    falling = coefficient[:, None, :] * jnp.exp(-rate[:, None, :] * steps[None, :, None])
    rising = jnp.exp(rate[:, :, None] * steps[None, None, :])
    lower = steps[:, None] >= steps[None, :]
    toeplitz = jnp.where(
        lower[None], jnp.einsum("gtm,gms->gts", falling, rising, precision=highest), 0.0
    )
    toe_hi = toeplitz.astype(jnp.bfloat16)
    toe_lo = (toeplitz - toe_hi.astype(jnp.float32)).astype(jnp.bfloat16)
    toe_both = jnp.concatenate([toe_hi, toe_lo], axis=2)
    x = gated.reshape(chunks, block, groups, group_width)
    docs_k = current.reshape(chunks, block)
    doc_ids = jnp.arange(n_docs, dtype=jnp.int32)
    in_doc = docs_k[None] == doc_ids[:, None, None]
    xd = jnp.where(in_doc[:, :, :, None, None], x[None], jnp.zeros((), jnp.bfloat16))
    xd = jnp.concatenate([xd, xd], axis=2)
    per_doc = jnp.einsum("gts,dksgc->dktgc", toe_both, xd, preferred_element_type=jnp.float32)
    intra = jnp.sum(jnp.where(in_doc[:, :, :, None, None], per_doc, 0.0), axis=0)

    x32 = x.astype(jnp.float32)
    ends_doc = docs_k[:, block - 1]
    at_end = (docs_k == ends_doc[:, None]).astype(jnp.float32)
    towards_end = jnp.exp(-rate[:, :, None] * (block - 1.0 - steps)[None, None, :])
    chunk_state = jnp.einsum(
        "gms,ksgc->kgmc", towards_end, x32 * at_end[:, :, None, None], precision=highest
    )
    chunk_ids = jnp.arange(chunks, dtype=jnp.int32)
    lag = (chunk_ids[:, None] - chunk_ids[None, :]).astype(jnp.float32)
    linked = (chunk_ids[:, None] >= chunk_ids[None, :]) & (ends_doc[:, None] == ends_doc[None, :])
    carry_weight = jnp.where(
        linked[:, :, None, None],
        jnp.exp(-rate[None, None] * (block * jnp.maximum(lag, 0.0))[:, :, None, None]),
        0.0,
    )
    local_state = jnp.sum(carry_weight[:, :, :, :, None] * chunk_state[None], axis=1)

    previous_doc = span_docs[1]
    gathered = lax.all_gather(local_state[chunks - 1], "ch")
    span_ids = jnp.arange(n_ch, dtype=jnp.int32)
    span_end_doc = doc_index((span_ids + 1) * span - 1, bounds)
    distance = jnp.maximum(here_ch - 1 - span_ids, 0).astype(jnp.float32)
    counted = (span_ids < here_ch) & (span_end_doc == previous_doc)
    span_weight = jnp.where(
        counted[:, None, None], jnp.exp(-rate[None] * (float(span) * distance)[:, None, None]), 0.0
    )
    entering = jnp.sum(span_weight[..., None] * gathered, axis=0)

    reach = jnp.exp(-rate[None] * (block * (chunk_ids + 1.0))[:, None, None])
    joined = (previous_doc == ends_doc).astype(jnp.float32)[:, None, None, None]
    total_state = local_state + reach[..., None] * joined * entering[None]
    before = jnp.concatenate([entering[None], total_state[: chunks - 1]], axis=0)
    start_prev_doc = jnp.concatenate([previous_doc[None], docs_k[: chunks - 1, block - 1]])
    from_before = (docs_k == start_prev_doc[:, None]).astype(jnp.float32)
    decaying = coefficient[:, None, :] * jnp.exp(-rate[:, None, :] * (steps + 1.0)[None, :, None])
    incoming = jnp.einsum("gtm,kgmc->ktgc", decaying, before, precision=highest)
    filtered = intra + incoming * from_before[:, :, None, None]

    gated32 = gated.astype(jnp.float32)
    combined = filtered.reshape(span, width) + skip[None, :] * gated32
    _, query_part = lax.optimization_barrier((arrived[0], projections[0:1]))
    (query_rows,) = arrive(query_part)
    mixed = (feature(0, query_rows) * combined).astype(jnp.bfloat16)

    back = jnp.dot(placer.T, mixed, preferred_element_type=jnp.float32).astype(jnp.bfloat16)
    returned = lax.all_to_all(back.reshape(n_ctx, rows_here, width), "ctx", 0, 0, tiled=True)
    return jnp.transpose(returned, (1, 0, 2)).reshape(rows_here, n_ctx * width)


def solution(mesh):
    placed = (
        P(None, ("ctx", "ch"), None),
        P(),
        P(),
        P(None, None, "ch"),
        P("ch", None),
        P("ch", None),
        P("ch"),
    )
    return jax.shard_map(layer, mesh=mesh, in_specs=placed, out_specs=P(("ctx", "ch"), None), check_vma=False)
```

```python
import jax
import jax.numpy as jnp
from jax import lax
from jax.sharding import PartitionSpec as P


highest = lax.Precision.HIGHEST


def doc_index(positions, bounds):
    found = jnp.sum((positions[:, None] >= bounds[None, :]).astype(jnp.int32), axis=1)
    return jnp.where(positions >= 0, found, -1)


def layer(projections, attention_order, doc_lengths, short_filter, decay_rate, residue, skip_gain):
    n_ctx = lax.axis_size("ctx")
    n_ch = lax.axis_size("ch")
    here_ctx = lax.axis_index("ctx")
    here_ch = lax.axis_index("ch")
    _, rows_here, channels = projections.shape
    tokens = attention_order.shape[0]
    block = tokens // n_ctx
    slot = block // n_ctx
    chunks = rows_here // slot
    span = chunks * block
    width = channels // n_ctx
    local_groups, modes = decay_rate.shape
    local_channels = short_filter.shape[2]
    group_width = local_channels // local_groups
    groups = width // group_width
    n_docs = doc_lengths.shape[0]

    sizes = (short_filter.size, decay_rate.size, residue.size, skip_gain.size)
    flat = jnp.concatenate(
        [short_filter.reshape(-1), decay_rate.reshape(-1), residue.reshape(-1), skip_gain.reshape(-1)]
    )
    every = lax.all_gather(flat, "ch")
    o1 = sizes[0]
    o2 = o1 + sizes[1]
    o3 = o2 + sizes[2]
    sf_all = jnp.transpose(every[:, :o1].reshape(n_ch, 3, 3, local_channels), (1, 2, 0, 3)).reshape(
        3, 3, n_ch * local_channels
    )
    sf = lax.dynamic_slice_in_dim(sf_all, here_ctx * width, width, 2)
    rate = lax.dynamic_slice_in_dim(every[:, o1:o2].reshape(n_ch * local_groups, modes), here_ctx * groups, groups, 0)
    res = lax.dynamic_slice_in_dim(every[:, o2:o3].reshape(n_ch * local_groups, modes), here_ctx * groups, groups, 0)
    skip = lax.dynamic_slice_in_dim(every[:, o3:].reshape(n_ch * local_channels), here_ctx * width, width, 0)
    coefficient = res * jnp.sqrt(1.0 - jnp.exp(-2.0 * rate))

    routing = attention_order.reshape(n_ctx, tokens // n_ctx)
    mine = lax.dynamic_slice_in_dim(routing, here_ch * rows_here, rows_here, 1).reshape(n_ctx * rows_here)
    placer = (
        (mine - here_ch * span)[None, :] == jnp.arange(span, dtype=jnp.int32)[:, None]
    ).astype(jnp.bfloat16)

    arrived = []

    def arrive(sending):
        count = sending.shape[1]
        received = lax.all_to_all(sending, "ctx", 0, 0, tiled=True)
        arrived.append(received)
        by_source = placer.reshape(span, n_ctx, rows_here)
        ordered = jnp.einsum(
            "tbr,bprc->ptc", by_source, received, preferred_element_type=jnp.float32
        ).astype(jnp.bfloat16)
        tail = jnp.einsum(
            "tbr,bprc->ptc", by_source[span - 2 :], received, preferred_element_type=jnp.float32
        ).astype(jnp.bfloat16)
        earlier = lax.ppermute(tail, "ch", [(i, i + 1) for i in range(n_ch - 1)])
        widened = jnp.concatenate([earlier, ordered], axis=1).astype(jnp.float32)
        return [widened[p] for p in range(count)]

    def outgoing(part):
        count = part.shape[0]
        return jnp.transpose(part.reshape(count, rows_here, n_ctx, width), (2, 0, 1, 3))

    bounds = jnp.cumsum(doc_lengths).astype(jnp.int32)
    span_docs = doc_index(here_ch * span - 2 + jnp.arange(span + 2, dtype=jnp.int32), bounds)
    current = span_docs[2:]
    keep_one = (span_docs[1 : 1 + span] == current).astype(jnp.float32)[:, None]
    keep_two = (span_docs[0:span] == current).astype(jnp.float32)[:, None]

    def feature(p, rows):
        return (
            sf[p, 0, None, :] * rows[2:]
            + sf[p, 1, None, :] * rows[1 : 1 + span] * keep_one
            + sf[p, 2, None, :] * rows[0:span] * keep_two
        )

    key_rows, value_rows = arrive(outgoing(projections[1:3]))
    featured_key = feature(1, key_rows)
    featured_value = feature(2, value_rows)
    gated = (featured_key * featured_value).astype(jnp.bfloat16)

    steps = jnp.arange(block, dtype=jnp.float32)
    falling = coefficient[:, None, :] * jnp.exp(-rate[:, None, :] * steps[None, :, None])
    rising = jnp.exp(rate[:, :, None] * steps[None, None, :])
    lower = steps[:, None] >= steps[None, :]
    toeplitz = jnp.where(
        lower[None], jnp.einsum("gtm,gms->gts", falling, rising, precision=highest), 0.0
    )
    toe_hi = toeplitz.astype(jnp.bfloat16)
    toe_lo = (toeplitz - toe_hi.astype(jnp.float32)).astype(jnp.bfloat16)
    toe_both = jnp.concatenate([toe_hi, toe_lo], axis=2)
    x = gated.reshape(chunks, block, groups, group_width)
    docs_k = current.reshape(chunks, block)
    doc_ids = jnp.arange(n_docs, dtype=jnp.int32)
    in_doc = docs_k[None] == doc_ids[:, None, None]
    xd = jnp.where(in_doc[:, :, :, None, None], x[None], jnp.zeros((), jnp.bfloat16))
    xd = jnp.concatenate([xd, xd], axis=2)
    per_doc = jnp.einsum("gts,dksgc->dktgc", toe_both, xd, preferred_element_type=jnp.float32)
    intra = jnp.sum(jnp.where(in_doc[:, :, :, None, None], per_doc, 0.0), axis=0)

    x32 = x.astype(jnp.float32)
    ends_doc = docs_k[:, block - 1]
    at_end = (docs_k == ends_doc[:, None]).astype(jnp.float32)
    towards_end = jnp.exp(-rate[:, :, None] * (block - 1.0 - steps)[None, None, :])
    chunk_state = jnp.einsum(
        "gms,ksgc->kgmc", towards_end, x32 * at_end[:, :, None, None], precision=highest
    )
    chunk_ids = jnp.arange(chunks, dtype=jnp.int32)
    lag = (chunk_ids[:, None] - chunk_ids[None, :]).astype(jnp.float32)
    linked = (chunk_ids[:, None] >= chunk_ids[None, :]) & (ends_doc[:, None] == ends_doc[None, :])
    carry_weight = jnp.where(
        linked[:, :, None, None],
        jnp.exp(-rate[None, None] * (block * jnp.maximum(lag, 0.0))[:, :, None, None]),
        0.0,
    )
    local_state = jnp.sum(carry_weight[:, :, :, :, None] * chunk_state[None], axis=1)

    previous_doc = span_docs[1]
    gathered = lax.all_gather(local_state[chunks - 1], "ch")
    span_ids = jnp.arange(n_ch, dtype=jnp.int32)
    span_end_doc = doc_index((span_ids + 1) * span - 1, bounds)
    distance = jnp.maximum(here_ch - 1 - span_ids, 0).astype(jnp.float32)
    counted = (span_ids < here_ch) & (span_end_doc == previous_doc)
    span_weight = jnp.where(
        counted[:, None, None], jnp.exp(-rate[None] * (float(span) * distance)[:, None, None]), 0.0
    )
    entering = jnp.sum(span_weight[..., None] * gathered, axis=0)

    reach = jnp.exp(-rate[None] * (block * (chunk_ids + 1.0))[:, None, None])
    joined = (previous_doc == ends_doc).astype(jnp.float32)[:, None, None, None]
    total_state = local_state + reach[..., None] * joined * entering[None]
    before = jnp.concatenate([entering[None], total_state[: chunks - 1]], axis=0)
    start_prev_doc = jnp.concatenate([previous_doc[None], docs_k[: chunks - 1, block - 1]])
    from_before = (docs_k == start_prev_doc[:, None]).astype(jnp.float32)
    decaying = coefficient[:, None, :] * jnp.exp(-rate[:, None, :] * (steps + 1.0)[None, :, None])
    incoming = jnp.einsum("gtm,kgmc->ktgc", decaying, before, precision=highest)
    filtered = intra + incoming * from_before[:, :, None, None]

    gated32 = gated.astype(jnp.float32)
    combined = filtered.reshape(span, width) + skip[None, :] * gated32
    _, query_sending = lax.optimization_barrier((arrived[0], outgoing(projections[0:1])))
    (query_rows,) = arrive(query_sending)
    mixed = (feature(0, query_rows) * combined).astype(jnp.bfloat16)

    back = jnp.dot(placer.T, mixed, preferred_element_type=jnp.float32).astype(jnp.bfloat16)
    returned = lax.all_to_all(back.reshape(n_ctx, rows_here, width), "ctx", 0, 0, tiled=True)
    return jnp.transpose(returned, (1, 0, 2)).reshape(rows_here, n_ctx * width)


def solution(mesh):
    placed = (
        P(None, ("ctx", "ch"), None),
        P(),
        P(),
        P(None, None, "ch"),
        P("ch", None),
        P("ch", None),
        P("ch"),
    )
    return jax.shard_map(layer, mesh=mesh, in_specs=placed, out_specs=P(("ctx", "ch"), None), check_vma=False)
```

```python
import jax
import jax.numpy as jnp
from jax import lax
from jax.sharding import PartitionSpec as P


highest = lax.Precision.HIGHEST


def doc_index(positions, bounds):
    found = jnp.sum((positions[:, None] >= bounds[None, :]).astype(jnp.int32), axis=1)
    return jnp.where(positions >= 0, found, -1)


def layer(projections, attention_order, doc_lengths, short_filter, decay_rate, residue, skip_gain):
    n_ctx = lax.axis_size("ctx")
    n_ch = lax.axis_size("ch")
    here_ctx = lax.axis_index("ctx")
    here_ch = lax.axis_index("ch")
    _, rows_here, channels = projections.shape
    tokens = attention_order.shape[0]
    block = tokens // n_ctx
    slot = block // n_ctx
    chunks = rows_here // slot
    span = chunks * block
    width = channels // n_ctx
    local_groups, modes = decay_rate.shape
    local_channels = short_filter.shape[2]
    group_width = local_channels // local_groups
    groups = width // group_width
    n_docs = doc_lengths.shape[0]

    sizes = (short_filter.size, decay_rate.size, residue.size, skip_gain.size)
    flat = jnp.concatenate(
        [short_filter.reshape(-1), decay_rate.reshape(-1), residue.reshape(-1), skip_gain.reshape(-1)]
    )
    every = lax.all_gather(flat, "ch")
    o1 = sizes[0]
    o2 = o1 + sizes[1]
    o3 = o2 + sizes[2]
    sf_all = jnp.transpose(every[:, :o1].reshape(n_ch, 3, 3, local_channels), (1, 2, 0, 3)).reshape(
        3, 3, n_ch * local_channels
    )
    sf = lax.dynamic_slice_in_dim(sf_all, here_ctx * width, width, 2)
    rate = lax.dynamic_slice_in_dim(every[:, o1:o2].reshape(n_ch * local_groups, modes), here_ctx * groups, groups, 0)
    res = lax.dynamic_slice_in_dim(every[:, o2:o3].reshape(n_ch * local_groups, modes), here_ctx * groups, groups, 0)
    skip = lax.dynamic_slice_in_dim(every[:, o3:].reshape(n_ch * local_channels), here_ctx * width, width, 0)
    coefficient = res * jnp.sqrt(1.0 - jnp.exp(-2.0 * rate))

    routing = attention_order.reshape(n_ctx, tokens // n_ctx)
    mine = lax.dynamic_slice_in_dim(routing, here_ch * rows_here, rows_here, 1).reshape(n_ctx * rows_here)
    placer = (
        (mine - here_ch * span)[None, :] == jnp.arange(span, dtype=jnp.int32)[:, None]
    ).astype(jnp.bfloat16)

    arrived = []

    def outgoing(part):
        count = part.shape[0]
        sending = jnp.transpose(part.reshape(count, rows_here, n_ctx, width), (2, 1, 0, 3))
        return sending.reshape(n_ctx, rows_here, count * width)

    def arrive(sending):
        count = sending.shape[2] // width
        received = lax.all_to_all(sending, "ctx", 0, 0, tiled=True)
        received = received.reshape(n_ctx * rows_here, count * width)
        arrived.append(received)
        ordered = jnp.dot(placer, received, preferred_element_type=jnp.float32).astype(jnp.bfloat16)
        tail = jnp.dot(placer[span - 2 :], received, preferred_element_type=jnp.float32).astype(jnp.bfloat16)
        earlier = lax.ppermute(tail, "ch", [(i, i + 1) for i in range(n_ch - 1)])
        widened = jnp.concatenate([earlier, ordered], axis=0).astype(jnp.float32)
        return [widened[:, p * width : (p + 1) * width] for p in range(count)]

    bounds = jnp.cumsum(doc_lengths).astype(jnp.int32)
    span_docs = doc_index(here_ch * span - 2 + jnp.arange(span + 2, dtype=jnp.int32), bounds)
    current = span_docs[2:]
    keep_one = (span_docs[1 : 1 + span] == current).astype(jnp.float32)[:, None]
    keep_two = (span_docs[0:span] == current).astype(jnp.float32)[:, None]

    def feature(p, rows):
        return (
            sf[p, 0, None, :] * rows[2:]
            + sf[p, 1, None, :] * rows[1 : 1 + span] * keep_one
            + sf[p, 2, None, :] * rows[0:span] * keep_two
        )

    key_rows, value_rows = arrive(outgoing(projections[1:3]))
    featured_key = feature(1, key_rows)
    featured_value = feature(2, value_rows)
    gated = (featured_key * featured_value).astype(jnp.bfloat16)

    steps = jnp.arange(block, dtype=jnp.float32)
    falling = coefficient[:, None, :] * jnp.exp(-rate[:, None, :] * steps[None, :, None])
    rising = jnp.exp(rate[:, :, None] * steps[None, None, :])
    lower = steps[:, None] >= steps[None, :]
    toeplitz = jnp.where(
        lower[None], jnp.einsum("gtm,gms->gts", falling, rising, precision=highest), 0.0
    )
    toe_hi = toeplitz.astype(jnp.bfloat16)
    toe_lo = (toeplitz - toe_hi.astype(jnp.float32)).astype(jnp.bfloat16)
    toe_both = jnp.concatenate([toe_hi, toe_lo], axis=2)
    x = gated.reshape(chunks, block, groups, group_width)
    docs_k = current.reshape(chunks, block)
    doc_ids = jnp.arange(n_docs, dtype=jnp.int32)
    in_doc = docs_k[None] == doc_ids[:, None, None]
    xd = jnp.where(in_doc[:, :, :, None, None], x[None], jnp.zeros((), jnp.bfloat16))
    xd = jnp.concatenate([xd, xd], axis=2)
    per_doc = jnp.einsum("gts,dksgc->dktgc", toe_both, xd, preferred_element_type=jnp.float32)
    intra = jnp.sum(jnp.where(in_doc[:, :, :, None, None], per_doc, 0.0), axis=0)

    x32 = x.astype(jnp.float32)
    ends_doc = docs_k[:, block - 1]
    at_end = (docs_k == ends_doc[:, None]).astype(jnp.float32)
    towards_end = jnp.exp(-rate[:, :, None] * (block - 1.0 - steps)[None, None, :])
    chunk_state = jnp.einsum(
        "gms,ksgc->kgmc", towards_end, x32 * at_end[:, :, None, None], precision=highest
    )
    chunk_ids = jnp.arange(chunks, dtype=jnp.int32)
    lag = (chunk_ids[:, None] - chunk_ids[None, :]).astype(jnp.float32)
    linked = (chunk_ids[:, None] >= chunk_ids[None, :]) & (ends_doc[:, None] == ends_doc[None, :])
    carry_weight = jnp.where(
        linked[:, :, None, None],
        jnp.exp(-rate[None, None] * (block * jnp.maximum(lag, 0.0))[:, :, None, None]),
        0.0,
    )
    local_state = jnp.sum(carry_weight[:, :, :, :, None] * chunk_state[None], axis=1)

    previous_doc = span_docs[1]
    gathered = lax.all_gather(local_state[chunks - 1], "ch")
    span_ids = jnp.arange(n_ch, dtype=jnp.int32)
    span_end_doc = doc_index((span_ids + 1) * span - 1, bounds)
    distance = jnp.maximum(here_ch - 1 - span_ids, 0).astype(jnp.float32)
    counted = (span_ids < here_ch) & (span_end_doc == previous_doc)
    span_weight = jnp.where(
        counted[:, None, None], jnp.exp(-rate[None] * (float(span) * distance)[:, None, None]), 0.0
    )
    entering = jnp.sum(span_weight[..., None] * gathered, axis=0)

    reach = jnp.exp(-rate[None] * (block * (chunk_ids + 1.0))[:, None, None])
    joined = (previous_doc == ends_doc).astype(jnp.float32)[:, None, None, None]
    total_state = local_state + reach[..., None] * joined * entering[None]
    before = jnp.concatenate([entering[None], total_state[: chunks - 1]], axis=0)
    start_prev_doc = jnp.concatenate([previous_doc[None], docs_k[: chunks - 1, block - 1]])
    from_before = (docs_k == start_prev_doc[:, None]).astype(jnp.float32)
    decaying = coefficient[:, None, :] * jnp.exp(-rate[:, None, :] * (steps + 1.0)[None, :, None])
    incoming = jnp.einsum("gtm,kgmc->ktgc", decaying, before, precision=highest)
    filtered = intra + incoming * from_before[:, :, None, None]

    gated32 = gated.astype(jnp.float32)
    combined = filtered.reshape(span, width) + skip[None, :] * gated32
    _, query_sending = lax.optimization_barrier((arrived[0], outgoing(projections[0:1])))
    (query_rows,) = arrive(query_sending)
    mixed = (feature(0, query_rows) * combined).astype(jnp.bfloat16)

    back = jnp.dot(placer.T, mixed, preferred_element_type=jnp.float32).astype(jnp.bfloat16)
    returned = lax.all_to_all(back.reshape(n_ctx, rows_here, width), "ctx", 0, 0, tiled=True)
    return jnp.transpose(returned, (1, 0, 2)).reshape(rows_here, n_ctx * width)


def solution(mesh):
    placed = (
        P(None, ("ctx", "ch"), None),
        P(),
        P(),
        P(None, None, "ch"),
        P("ch", None),
        P("ch", None),
        P("ch"),
    )
    return jax.shard_map(layer, mesh=mesh, in_specs=placed, out_specs=P(("ctx", "ch"), None), check_vma=False)
```

```python
import jax
import jax.numpy as jnp
from jax import lax
from jax.sharding import PartitionSpec as P


highest = lax.Precision.HIGHEST


def doc_index(positions, bounds):
    found = jnp.sum((positions[:, None] >= bounds[None, :]).astype(jnp.int32), axis=1)
    return jnp.where(positions >= 0, found, -1)


def layer(projections, attention_order, doc_lengths, short_filter, decay_rate, residue, skip_gain):
    n_ctx = lax.axis_size("ctx")
    n_ch = lax.axis_size("ch")
    here_ctx = lax.axis_index("ctx")
    here_ch = lax.axis_index("ch")
    _, rows_here, channels = projections.shape
    tokens = attention_order.shape[0]
    block = tokens // n_ctx
    slot = block // n_ctx
    chunks = rows_here // slot
    span = chunks * block
    width = channels // n_ctx
    local_groups, modes = decay_rate.shape
    local_channels = short_filter.shape[2]
    group_width = local_channels // local_groups
    groups = width // group_width
    n_docs = doc_lengths.shape[0]

    sizes = (short_filter.size, decay_rate.size, residue.size, skip_gain.size)
    flat = jnp.concatenate(
        [short_filter.reshape(-1), decay_rate.reshape(-1), residue.reshape(-1), skip_gain.reshape(-1)]
    )
    every = lax.all_gather(flat, "ch")
    o1 = sizes[0]
    o2 = o1 + sizes[1]
    o3 = o2 + sizes[2]
    sf_all = jnp.transpose(every[:, :o1].reshape(n_ch, 3, 3, local_channels), (1, 2, 0, 3)).reshape(
        3, 3, n_ch * local_channels
    )
    sf = lax.dynamic_slice_in_dim(sf_all, here_ctx * width, width, 2)
    rate = lax.dynamic_slice_in_dim(every[:, o1:o2].reshape(n_ch * local_groups, modes), here_ctx * groups, groups, 0)
    res = lax.dynamic_slice_in_dim(every[:, o2:o3].reshape(n_ch * local_groups, modes), here_ctx * groups, groups, 0)
    skip = lax.dynamic_slice_in_dim(every[:, o3:].reshape(n_ch * local_channels), here_ctx * width, width, 0)
    coefficient = res * jnp.sqrt(1.0 - jnp.exp(-2.0 * rate))

    routing = attention_order.reshape(n_ctx, tokens // n_ctx)
    mine = lax.dynamic_slice_in_dim(routing, here_ch * rows_here, rows_here, 1).reshape(n_ctx * rows_here)
    placer = (
        (mine - here_ch * span)[None, :] == jnp.arange(span, dtype=jnp.int32)[:, None]
    ).astype(jnp.bfloat16)

    arrived = []

    def arrive(part):
        count = part.shape[0]
        sending = jnp.transpose(part.reshape(count, rows_here, n_ctx, width), (2, 1, 0, 3))
        sending = sending.reshape(n_ctx, rows_here, count * width)
        received = lax.all_to_all(sending, "ctx", 0, 0, tiled=True)
        received = received.reshape(n_ctx * rows_here, count * width)
        arrived.append(received)
        ordered = jnp.dot(placer, received, preferred_element_type=jnp.bfloat16)
        tail = jnp.dot(placer[span - 2 :], received, preferred_element_type=jnp.bfloat16)
        earlier = lax.ppermute(tail, "ch", [(i, i + 1) for i in range(n_ch - 1)])
        widened = jnp.concatenate([earlier, ordered], axis=0).astype(jnp.float32)
        return [widened[:, p * width : (p + 1) * width] for p in range(count)]

    bounds = jnp.cumsum(doc_lengths).astype(jnp.int32)
    span_docs = doc_index(here_ch * span - 2 + jnp.arange(span + 2, dtype=jnp.int32), bounds)
    current = span_docs[2:]
    keep_one = (span_docs[1 : 1 + span] == current).astype(jnp.float32)[:, None]
    keep_two = (span_docs[0:span] == current).astype(jnp.float32)[:, None]

    def feature(p, rows):
        return (
            sf[p, 0, None, :] * rows[2:]
            + sf[p, 1, None, :] * rows[1 : 1 + span] * keep_one
            + sf[p, 2, None, :] * rows[0:span] * keep_two
        )

    key_rows, value_rows = arrive(projections[1:3])
    featured_key = feature(1, key_rows)
    featured_value = feature(2, value_rows)
    gated = (featured_key * featured_value).astype(jnp.bfloat16)

    steps = jnp.arange(block, dtype=jnp.float32)
    falling = coefficient[:, None, :] * jnp.exp(-rate[:, None, :] * steps[None, :, None])
    rising = jnp.exp(rate[:, :, None] * steps[None, None, :])
    lower = steps[:, None] >= steps[None, :]
    toeplitz = jnp.where(
        lower[None], jnp.einsum("gtm,gms->gts", falling, rising, precision=highest), 0.0
    )
    toe_hi = toeplitz.astype(jnp.bfloat16)
    toe_lo = (toeplitz - toe_hi.astype(jnp.float32)).astype(jnp.bfloat16)
    toe_both = jnp.concatenate([toe_hi, toe_lo], axis=2)
    x = gated.reshape(chunks, block, groups, group_width)
    docs_k = current.reshape(chunks, block)
    doc_ids = jnp.arange(n_docs, dtype=jnp.int32)
    in_doc = docs_k[None] == doc_ids[:, None, None]
    xd = jnp.where(in_doc[:, :, :, None, None], x[None], jnp.zeros((), jnp.bfloat16))
    xd = jnp.concatenate([xd, xd], axis=2)
    per_doc = jnp.einsum("gts,dksgc->dktgc", toe_both, xd, preferred_element_type=jnp.float32)
    intra = jnp.sum(jnp.where(in_doc[:, :, :, None, None], per_doc, 0.0), axis=0)

    x32 = x.astype(jnp.float32)
    ends_doc = docs_k[:, block - 1]
    at_end = (docs_k == ends_doc[:, None]).astype(jnp.float32)
    towards_end = jnp.exp(-rate[:, :, None] * (block - 1.0 - steps)[None, None, :])
    chunk_state = jnp.einsum(
        "gms,ksgc->kgmc", towards_end, x32 * at_end[:, :, None, None], precision=highest
    )
    chunk_ids = jnp.arange(chunks, dtype=jnp.int32)
    lag = (chunk_ids[:, None] - chunk_ids[None, :]).astype(jnp.float32)
    linked = (chunk_ids[:, None] >= chunk_ids[None, :]) & (ends_doc[:, None] == ends_doc[None, :])
    carry_weight = jnp.where(
        linked[:, :, None, None],
        jnp.exp(-rate[None, None] * (block * jnp.maximum(lag, 0.0))[:, :, None, None]),
        0.0,
    )
    local_state = jnp.sum(carry_weight[:, :, :, :, None] * chunk_state[None], axis=1)

    previous_doc = span_docs[1]
    gathered = lax.all_gather(local_state[chunks - 1], "ch")
    span_ids = jnp.arange(n_ch, dtype=jnp.int32)
    span_end_doc = doc_index((span_ids + 1) * span - 1, bounds)
    distance = jnp.maximum(here_ch - 1 - span_ids, 0).astype(jnp.float32)
    counted = (span_ids < here_ch) & (span_end_doc == previous_doc)
    span_weight = jnp.where(
        counted[:, None, None], jnp.exp(-rate[None] * (float(span) * distance)[:, None, None]), 0.0
    )
    entering = jnp.sum(span_weight[..., None] * gathered, axis=0)

    reach = jnp.exp(-rate[None] * (block * (chunk_ids + 1.0))[:, None, None])
    joined = (previous_doc == ends_doc).astype(jnp.float32)[:, None, None, None]
    total_state = local_state + reach[..., None] * joined * entering[None]
    before = jnp.concatenate([entering[None], total_state[: chunks - 1]], axis=0)
    start_prev_doc = jnp.concatenate([previous_doc[None], docs_k[: chunks - 1, block - 1]])
    from_before = (docs_k == start_prev_doc[:, None]).astype(jnp.float32)
    decaying = coefficient[:, None, :] * jnp.exp(-rate[:, None, :] * (steps + 1.0)[None, :, None])
    incoming = jnp.einsum("gtm,kgmc->ktgc", decaying, before, precision=highest)
    filtered = intra + incoming * from_before[:, :, None, None]

    gated32 = gated.astype(jnp.float32)
    combined = filtered.reshape(span, width) + skip[None, :] * gated32
    _, query_part = lax.optimization_barrier((arrived[0], projections[0:1]))
    (query_rows,) = arrive(query_part)
    mixed = (feature(0, query_rows) * combined).astype(jnp.bfloat16)

    back = jnp.dot(placer.T, mixed, preferred_element_type=jnp.bfloat16)
    returned = lax.all_to_all(back.reshape(n_ctx, rows_here, width), "ctx", 0, 0, tiled=True)
    return jnp.transpose(returned, (1, 0, 2)).reshape(rows_here, n_ctx * width)


def solution(mesh):
    placed = (
        P(None, ("ctx", "ch"), None),
        P(),
        P(),
        P(None, None, "ch"),
        P("ch", None),
        P("ch", None),
        P("ch"),
    )
    return jax.shard_map(layer, mesh=mesh, in_specs=placed, out_specs=P(("ctx", "ch"), None), check_vma=False)
```
